768 devices in a mesh: sub: 192 (over y, z, core), col: 4 (over x).
Axes of the slice: x: 4, y: 8, z: 12, core: 2. Of those that a mesh axis runs over, the one named last changes fastest.
Arguments:
- right_sides: float32 [64, 196608], P(None, ('sub', 'col')), may hold values from -6 to 6
- operator: float32 [192, 1536, 1024], P('sub', None, 'col'), may hold values from -0.15625 to 0.15625
- local_inverse: float32 [192, 1536, 1024], P('sub', None, 'col'), may hold values from -0.15625 to 0.15625
- coarse_basis: float32 [192, 1536, 64], P('sub'), may hold values from -0.15625 to 0.15625
- coarse_inverse: float32 [12288, 12288], P('sub', 'col'), may hold values from -0.15625 to 0.15625
- send_index: int32 [192, 4, 4, 32], P('sub', 'col'), may hold values from 0 to 255
- halo_count: int32 [192, 4, 4], P('sub', 'col'), may hold values from 1 to 32, as said below
Outputs:
- solution: float32 [64, 196608], P(None, ('sub', 'col'))
- residual: float32 [64, 196608], P(None, ('sub', 'col'))
The draws below stay inside these ranges and needn't reach their ends.
Inputs may be any that keep to these rules, and one draw needn't show every extreme that they name: `halo_count`: on every device of every draw at least one of its 4 counts equals 32.
All inputs are finite; a program needn't handle non-finite values.
Results may differ from the reference program's by a relative error of at most 0.000078.
Values sent between devices are 32-bit elements; how exact they have to be, the bound alone decides.
No kernel may reach another device: no remote copies, remote signals or barrier semaphores. Data moves between devices by JAX's collectives and lax.ppermute only.
A program may use at most 32 MiB of HBM per device.

```python
import jax
import jax.numpy as jnp
from jax import lax

NRHS = 64
EXT = 1536
MODES = 64
NB = 4
HB = 32
SUBS = 192
CH = 384
OWNC = 256
OWN = 1024
MQ = 16
NC = 12288
STRIDE = 48
N_COL = 4


def draw_halo_count(key, part):
    first_key, second_key = jax.random.split(key)
    counts = jax.random.randint(first_key, (SUBS, N_COL, NB), 1, HB + 1)
    which = jax.random.randint(second_key, (SUBS, N_COL, 1), 0, NB)
    slots = jnp.arange(NB, dtype=jnp.int32)[None, None, :]
    return jnp.where(slots == which, HB, counts).astype(jnp.int32)


def set_ends(entries, stream_key, smallest, high):
    longest = entries.shape.index(max(entries.shape))
    spots = []
    for shift in (0, 1):
        where = [jax.random.randint(jax.random.fold_in(stream_key, axis), (), 0, length) for axis, length in enumerate(entries.shape)]
        where[longest] = (where[longest] + shift) % entries.shape[longest]
        spots.append(tuple(where))
    return entries.at[spots[0]].set(smallest).at[spots[1]].set(high)


def block_levels(rng, dims, cuts, smallest, top_value):
    level = 1.0
    for position, shards_of in cuts:
        steps = jax.random.uniform(jax.random.fold_in(jax.random.fold_in(rng, 6), position), (shards_of,), jnp.float32, smallest / len(cuts), top_value / len(cuts))
        level = level * jnp.repeat(jnp.exp(steps), dims[position] // shards_of).reshape((-1,) + (1,) * (len(dims) - 1 - position))
    return level


def normal_values(stream_key, shape, width, limit, cuts=(), held_as=jnp.bfloat16):
    level = block_levels(stream_key, shape, cuts, -0.22, 0.18) if cuts else 1.0
    array = jax.random.normal(stream_key, shape, jnp.float32) * width * level
    return jnp.minimum(jnp.maximum(array, -limit), limit).astype(held_as)


def setup_inputs(seed: int = 0) -> dict:
    key_list = jax.random.split(jax.random.key(seed), 8)
    right_sides = normal_values(key_list[0], (NRHS, SUBS * OWN), 1.0, 6.0, ((1, 768),), jnp.float32)
    operator = normal_values(key_list[1], (SUBS, EXT, OWN), EXT ** -0.5, 0.15625, ((0, 192), (2, 4)), jnp.float32)
    local_inverse = normal_values(key_list[2], (SUBS, EXT, OWN), EXT ** -0.5, 0.15625, ((0, 192), (2, 4)), jnp.float32)
    coarse_basis = normal_values(key_list[3], (SUBS, EXT, MODES), EXT ** -0.5, 0.15625, ((0, 192),), jnp.float32)
    coarse_inverse = normal_values(key_list[4], (NC, NC), (NC // 8) ** -0.5, 0.15625, ((0, 192), (1, 4)), jnp.float32)
    send_index = set_ends(jax.random.randint(key_list[5], (SUBS, N_COL, NB, HB), 0, OWNC), jax.random.fold_in(key_list[5], 1), 0, OWNC - 1).astype(jnp.int32)
    halo_count = draw_halo_count(jax.random.fold_in(key_list[7], 71), 0)
    return dict(right_sides=right_sides, operator=operator, local_inverse=local_inverse, coarse_basis=coarse_basis, coarse_inverse=coarse_inverse, send_index=send_index, halo_count=halo_count)


HIGH = lax.Precision.HIGHEST


def shifted(packed, offset):
    blank_rows = jnp.zeros_like(packed[:, :abs(offset)])
    if offset > 0:
        return jnp.concatenate([blank_rows, packed[:, :-offset]], axis=1)
    return jnp.concatenate([packed[:, -offset:], blank_rows], axis=1)


def extended(field, send_index, halo_count):
    rhs_width = field.shape[0]
    own_rows = field.reshape(rhs_width, SUBS, N_COL, OWNC)
    slots = jnp.arange(HB, dtype=jnp.int32)
    live_slots = (slots[None, None, None, :] < halo_count[:, :, :, None]).astype(jnp.float32)
    pieces = [own_rows]
    for number, offset in enumerate((1, -1, STRIDE, -STRIDE)):
        chosen = jnp.broadcast_to(send_index[None, :, :, number, :], (rhs_width, SUBS, N_COL, HB)).astype(jnp.int32)
        packed = jnp.take_along_axis(own_rows, chosen, axis=3) * live_slots[None, :, :, number, :]
        pieces.append(shifted(packed, offset))
    return jnp.concatenate(pieces, axis=3).reshape(rhs_width, SUBS, EXT)


def precondition(field, local_inverse, coarse_basis, coarse_inverse, send_index, halo_count):
    rhs_width = field.shape[0]
    extension = extended(field, send_index, halo_count)
    local_part = jnp.einsum("rse,seo->rso", extension, local_inverse, precision=HIGH)
    mode_coeffs = jnp.einsum("rse,sem->smr", extension, coarse_basis, precision=HIGH)
    ordered = mode_coeffs.reshape(SUBS, N_COL, MQ, rhs_width).transpose(1, 0, 2, 3).reshape(NC, rhs_width)
    coarse_vals = jnp.dot(coarse_inverse, ordered, precision=HIGH).reshape(SUBS, MODES, rhs_width)
    own_basis = coarse_basis.reshape(SUBS, N_COL, CH, MODES)[:, :, :OWNC].reshape(SUBS, OWN, MODES)
    coarse_part = jnp.einsum("smr,som->rso", coarse_vals, own_basis, precision=HIGH)
    return (local_part + coarse_part).reshape(rhs_width, SUBS * OWN)


def reference(right_sides, operator, local_inverse, coarse_basis, coarse_inverse, send_index, halo_count):
    rhs_width = right_sides.shape[0]
    first_pass = precondition(right_sides, local_inverse, coarse_basis, coarse_inverse, send_index, halo_count)
    extension = extended(first_pass, send_index, halo_count)
    applied = jnp.einsum("rse,seo->rso", extension, operator, precision=HIGH).reshape(rhs_width, SUBS * OWN)
    residual = right_sides - applied
    solution = first_pass + precondition(residual, local_inverse, coarse_basis, coarse_inverse, send_index, halo_count)
    return (solution, residual)
```

```python
import jax
import jax.numpy as jnp
from jax import lax
from jax.sharding import Mesh, PartitionSpec as P

HIGH = lax.Precision.HIGHEST
CORES = 2
ZLEN = 12
SUB = ("y", "z", "core")


def passed_along(block, distance, subs):
    route = [(i - distance, i) for i in range(subs) if 0 <= i - distance < subs]
    return lax.ppermute(block, SUB, route)


def body(
    right_sides, operator, local_inverse, coarse_basis, coarse_inverse, send_index, halo_count
):
    own_width = right_sides.shape[1]
    rhs_width = right_sides.shape[0]
    halo_slots = send_index.shape[3]
    n_col = lax.axis_size("col")
    subs = lax.axis_size("y") * ZLEN * CORES
    stride = subs // 4
    offsets = (1, -1, stride, -stride)
    send_rows = send_index[0, 0]
    counts = halo_count[0, 0]
    live_slots = (jnp.arange(halo_slots, dtype=jnp.int32)[None, :] < counts[:, None]).astype(
        jnp.float32
    )
    operator_rows = operator[0]
    inverse_rows = local_inverse[0]
    basis_rows = coarse_basis[0]
    mode_count = basis_rows.shape[1]
    block_len = basis_rows.shape[0] // n_col
    column_index = lax.axis_index("col")
    quarter = mode_count // n_col

    def extend_apply(field, matrices):
        pieces = [field]
        for number in range(len(offsets)):
            packed = jnp.take(field, send_rows[number], axis=1) * live_slots[number][None, :]
            pieces.append(passed_along(packed, offsets[number], subs))
        own_and_halo = jnp.concatenate(pieces, axis=1)
        segment = lax.all_gather(own_and_halo, "col", axis=1, tiled=True)
        return tuple([jnp.dot(segment, matrix, precision=HIGH) for matrix in matrices])

    def precondition(field):
        local_part, coeff_rows = extend_apply(field, (inverse_rows, basis_rows))
        mode_coeffs = coeff_rows.T
        mine = lax.dynamic_slice_in_dim(mode_coeffs, column_index * quarter, quarter, 0)
        row = lax.all_gather(mine[None], ("z", "core"), axis=0, tiled=True)
        kept_rows = lax.all_gather(row, "y", axis=0, tiled=True).reshape(
            subs * quarter, rhs_width
        )
        partial_sum = jnp.dot(coarse_inverse, kept_rows, precision=HIGH)
        every = lax.all_gather(partial_sum[None], "col", axis=0, tiled=True)
        coarse_vals = jnp.sum(every, axis=0)
        own_basis = lax.dynamic_slice_in_dim(basis_rows, column_index * block_len, own_width, 0)
        coarse_part = lax.dot_general(
            coarse_vals, own_basis, (((0,), (1,)), ((), ())), precision=HIGH
        )
        return local_part + coarse_part

    first_pass = precondition(right_sides)
    applied_parts = extend_apply(first_pass, (operator_rows,))
    residual = right_sides - applied_parts[0]
    solution = first_pass + precondition(residual)
    return (solution, residual)


def solution(mesh):
    subs, n_col = mesh.devices.shape
    fine = Mesh(
        mesh.devices.reshape(subs // (ZLEN * CORES), ZLEN, CORES, n_col), SUB + ("col",)
    )
    placed = (
        P(None, SUB + ("col",)),
        P(SUB, None, "col"),
        P(SUB, None, "col"),
        P(SUB, None, None),
        P(SUB, "col"),
        P(SUB, "col", None, None),
        P(SUB, "col", None),
    )
    return jax.shard_map(
        body,
        mesh=fine,
        in_specs=placed,
        out_specs=(P(None, SUB + ("col",)), P(None, SUB + ("col",))),
        check_vma=False,
    )
```

```python
import jax
import jax.numpy as jnp
from jax import lax
from jax.sharding import Mesh, PartitionSpec as P

HIGH = lax.Precision.HIGHEST
CORES = 2
ZLEN = 12
SUB = ("y", "z", "core")


def passed_along(block, distance, subs):
    route = [(i - distance, i) for i in range(subs) if 0 <= i - distance < subs]
    return lax.ppermute(block, SUB, route)


def body(
    right_sides, operator, local_inverse, coarse_basis, coarse_inverse, send_index, halo_count
):
    own_width = right_sides.shape[1]
    rhs_width = right_sides.shape[0]
    halo_slots = send_index.shape[3]
    n_nb = send_index.shape[2]
    n_col = lax.axis_size("col")
    ylen = lax.axis_size("y")
    subs = ylen * ZLEN * CORES
    stride = subs // 4
    offsets = (1, -1, stride, -stride)
    send_rows = send_index[0, 0]
    counts = halo_count[0, 0]
    slots = jnp.arange(halo_slots, dtype=jnp.int32)
    live_slots = (slots[None, :] < counts[:, None]).astype(jnp.float32)
    basis_rows = coarse_basis[0]
    mode_count = basis_rows.shape[1]
    block_len = basis_rows.shape[0] // n_col
    blocks_of = lambda m: m.reshape(n_col, block_len, m.shape[-1])
    operator_rows = blocks_of(operator[0])
    inverse_rows = blocks_of(local_inverse[0])
    basis_blocks = blocks_of(basis_rows)
    own_basis_all = basis_blocks[:, :own_width]
    column_index = lax.axis_index("col")
    quarter = mode_count // n_col
    own_basis = lax.dynamic_index_in_dim(own_basis_all, column_index, 0, keepdims=False)

    def pack_own(field):
        packed = [
            jnp.take(field, send_rows[n], axis=1) * live_slots[n][None, :] for n in range(n_nb)
        ]
        return jnp.concatenate(packed, axis=1)

    def halos(packs):
        got = [passed_along(packs[:, :, n], offsets[n], subs) for n in range(n_nb)]
        return got

    def ext_of(own_all, got):
        return jnp.concatenate([own_all] + got, axis=2)

    def apply(ext, blocks):
        return lax.dot_general(ext, blocks, (((0, 2), (0, 1)), ((), ())), precision=HIGH)

    def gathered_ext(field, extra=None):
        payload = jnp.concatenate([field, pack_own(field)], axis=1)
        if extra is not None:
            payload = jnp.concatenate([payload, extra], axis=0)
        g = lax.all_gather(payload[None], "col", axis=0, tiled=True)
        own_all = g[:, :rhs_width, :own_width]
        packs = g[:, :rhs_width, own_width:].reshape(n_col, rhs_width, n_nb, halo_slots)
        return ext_of(own_all, halos(packs)), g[:, rhs_width:]

    def coarse_partial(ext):
        coeff = apply(ext, basis_blocks)
        mine = lax.dynamic_slice_in_dim(coeff, column_index * quarter, quarter, 1).T
        g = lax.all_gather(mine[None], "z", axis=0, tiled=True)
        g = lax.all_gather(g[None], ("y", "core"), axis=0, tiled=True)
        g = g.reshape(ylen, CORES, ZLEN, quarter, rhs_width).transpose(0, 2, 1, 3, 4)
        kept_rows = g.reshape(subs * quarter, rhs_width)
        return jnp.dot(coarse_inverse, kept_rows, precision=HIGH)

    index_row = jnp.concatenate(
        [
            send_rows.reshape(-1).astype(jnp.float32),
            counts.astype(jnp.float32),
            jnp.zeros((own_width + n_nb * halo_slots - n_nb * halo_slots - n_nb,), jnp.float32),
        ]
    )[None]
    ext_b, idx = gathered_ext(right_sides, index_row)
    send_all = idx[:, 0, : n_nb * halo_slots].astype(jnp.int32).reshape(n_col, n_nb, halo_slots)
    counts_all = idx[:, 0, n_nb * halo_slots : n_nb * halo_slots + n_nb].astype(jnp.int32)
    live_all = (slots[None, None, :] < counts_all[:, :, None]).astype(jnp.float32)

    local_1 = apply(ext_b, inverse_rows)
    partial_1 = coarse_partial(ext_b)
    g = lax.all_gather(
        jnp.concatenate([local_1, partial_1.T], axis=1)[None], "col", axis=0, tiled=True
    )
    local_all = g[:, :, :own_width]
    coarse_1 = jnp.sum(g[:, :, own_width:], axis=0)
    coarse_part_all = jnp.einsum("rm,com->cro", coarse_1, own_basis_all, precision=HIGH)
    first_all = local_all + coarse_part_all
    packs_first = jnp.stack(
        [
            jnp.take_along_axis(first_all, send_all[:, n][:, None, :], axis=2)
            * live_all[:, n][:, None, :]
            for n in range(n_nb)
        ],
        axis=2,
    )
    ext_f = ext_of(first_all, halos(packs_first))
    applied = apply(ext_f, operator_rows)
    residual = right_sides - applied
    first_pass = lax.dynamic_index_in_dim(first_all, column_index, 0, keepdims=False)

    ext_r, _ = gathered_ext(residual)
    local_2 = apply(ext_r, inverse_rows)
    partial_2 = coarse_partial(ext_r)
    g2 = lax.all_gather(partial_2.T[None], "col", axis=0, tiled=True)
    coarse_2 = jnp.sum(g2, axis=0)
    coarse_part_2 = lax.dot_general(
        coarse_2, own_basis, (((1,), (1,)), ((), ())), precision=HIGH
    )
    solution = first_pass + (local_2 + coarse_part_2)
    return (solution, residual)


def solution(mesh):
    subs, n_col = mesh.devices.shape
    fine = Mesh(
        mesh.devices.reshape(subs // (ZLEN * CORES), ZLEN, CORES, n_col), SUB + ("col",)
    )
    placed = (
        P(None, SUB + ("col",)),
        P(SUB, None, "col"),
        P(SUB, None, "col"),
        P(SUB, None, None),
        P(SUB, "col"),
        P(SUB, "col", None, None),
        P(SUB, "col", None),
    )
    return jax.shard_map(
        body,
        mesh=fine,
        in_specs=placed,
        out_specs=(P(None, SUB + ("col",)), P(None, SUB + ("col",))),
        check_vma=False,
    )
```

```python
import jax
import jax.numpy as jnp
from jax import lax
from jax.sharding import Mesh, PartitionSpec as P

HIGH = lax.Precision.HIGHEST
CORES = 2
ZLEN = 12
SUB = ("y", "z", "core")


def passed_along(block, distance, subs):
    route = [(i - distance, i) for i in range(subs) if 0 <= i - distance < subs]
    return lax.ppermute(block, SUB, route)


def body(
    right_sides, operator, local_inverse, coarse_basis, coarse_inverse, send_index, halo_count
):
    own_width = right_sides.shape[1]
    rhs_width = right_sides.shape[0]
    halo_slots = send_index.shape[3]
    n_nb = send_index.shape[2]
    n_col = lax.axis_size("col")
    ylen = lax.axis_size("y")
    subs = ylen * ZLEN * CORES
    stride = subs // 4
    offsets = (1, -1, stride, -stride)
    send_rows = send_index[0, 0]
    counts = halo_count[0, 0]
    slots = jnp.arange(halo_slots, dtype=jnp.int32)
    live_slots = (slots[None, :] < counts[:, None]).astype(jnp.float32)
    basis_rows = coarse_basis[0]
    mode_count = basis_rows.shape[1]
    block_len = basis_rows.shape[0] // n_col
    blocks_of = lambda m: m.reshape(n_col, block_len, m.shape[-1])
    operator_rows = blocks_of(operator[0])
    inverse_rows = blocks_of(local_inverse[0])
    basis_blocks = blocks_of(basis_rows)
    own_basis_all = basis_blocks[:, :own_width]
    column_index = lax.axis_index("col")
    quarter = mode_count // n_col
    own_basis = lax.dynamic_index_in_dim(own_basis_all, column_index, 0, keepdims=False)
    rows = jnp.arange(own_width, dtype=jnp.int32)
    select_own = (
        (rows[:, None, None] == send_rows[None]).astype(jnp.float32) * live_slots[None]
    ).reshape(own_width, n_nb * halo_slots)

    def pack_own(field):
        return jnp.dot(field, select_own, precision=HIGH)

    def halos(packs):
        got = [passed_along(packs[:, :, n], offsets[n], subs) for n in range(n_nb)]
        return got

    def ext_of(own_all, got):
        return jnp.concatenate([own_all] + got, axis=2)

    def apply(ext, blocks):
        return lax.dot_general(ext, blocks, (((0, 2), (0, 1)), ((), ())), precision=HIGH)

    def gathered_ext(field, extra=None):
        payload = jnp.concatenate([field, pack_own(field)], axis=1)
        if extra is not None:
            payload = jnp.concatenate([payload, extra], axis=0)
        g = lax.all_gather(payload[None], "col", axis=0, tiled=True)
        own_all = g[:, :rhs_width, :own_width]
        packs = g[:, :rhs_width, own_width:].reshape(n_col, rhs_width, n_nb, halo_slots)
        return ext_of(own_all, halos(packs)), g[:, rhs_width:]

    def coarse_partial(ext):
        coeff = apply(ext, basis_blocks)
        mine = lax.dynamic_slice_in_dim(coeff, column_index * quarter, quarter, 1).T
        g = lax.all_gather(mine[None], "z", axis=0, tiled=True)
        g = lax.all_gather(g[None], ("y", "core"), axis=0, tiled=True)
        g = g.reshape(ylen, CORES, ZLEN, quarter, rhs_width).transpose(0, 2, 1, 3, 4)
        kept_rows = g.reshape(subs * quarter, rhs_width)
        return jnp.dot(coarse_inverse, kept_rows, precision=HIGH)

    index_row = jnp.concatenate(
        [
            send_rows.reshape(-1).astype(jnp.float32),
            counts.astype(jnp.float32),
            jnp.zeros((own_width + n_nb * halo_slots - n_nb * halo_slots - n_nb,), jnp.float32),
        ]
    )[None]
    ext_b, idx = gathered_ext(right_sides, index_row)
    send_all = idx[:, 0, : n_nb * halo_slots].astype(jnp.int32).reshape(n_col, n_nb, halo_slots)
    counts_all = idx[:, 0, n_nb * halo_slots : n_nb * halo_slots + n_nb].astype(jnp.int32)
    live_all = (slots[None, None, :] < counts_all[:, :, None]).astype(jnp.float32)

    local_1 = apply(ext_b, inverse_rows)
    partial_1 = coarse_partial(ext_b)
    g = lax.all_gather(
        jnp.concatenate([local_1, partial_1.T], axis=1)[None], "col", axis=0, tiled=True
    )
    local_all = g[:, :, :own_width]
    coarse_1 = jnp.sum(g[:, :, own_width:], axis=0)
    coarse_part_all = jnp.einsum("rm,com->cro", coarse_1, own_basis_all, precision=HIGH)
    first_all = local_all + coarse_part_all
    select_all = (rows[None, :, None, None] == send_all[:, None]).astype(jnp.float32) * live_all[
        :, None
    ]
    got_first = [
        passed_along(
            lax.dot_general(
                first_all, select_all[:, :, n], (((2,), (1,)), ((0,), (0,))), precision=HIGH
            ),
            offsets[n],
            subs,
        )
        for n in range(n_nb)
    ]
    ext_f = ext_of(first_all, got_first)
    applied = apply(ext_f, operator_rows)
    residual = right_sides - applied
    first_pass = lax.dynamic_index_in_dim(first_all, column_index, 0, keepdims=False)

    ext_r, _ = gathered_ext(residual)
    local_2 = apply(ext_r, inverse_rows)
    partial_2 = coarse_partial(ext_r)
    g2 = lax.all_gather(partial_2.T[None], "col", axis=0, tiled=True)
    coarse_2 = jnp.sum(g2, axis=0)
    coarse_part_2 = lax.dot_general(
        coarse_2, own_basis, (((1,), (1,)), ((), ())), precision=HIGH
    )
    solution = first_pass + (local_2 + coarse_part_2)
    return (solution, residual)


def solution(mesh):
    subs, n_col = mesh.devices.shape
    fine = Mesh(
        mesh.devices.reshape(subs // (ZLEN * CORES), ZLEN, CORES, n_col), SUB + ("col",)
    )
    placed = (
        P(None, SUB + ("col",)),
        P(SUB, None, "col"),
        P(SUB, None, "col"),
        P(SUB, None, None),
        P(SUB, "col"),
        P(SUB, "col", None, None),
        P(SUB, "col", None),
    )
    return jax.shard_map(
        body,
        mesh=fine,
        in_specs=placed,
        out_specs=(P(None, SUB + ("col",)), P(None, SUB + ("col",))),
        check_vma=False,
    )
```

```python
import jax
import jax.numpy as jnp
from jax import lax
from jax.sharding import Mesh, PartitionSpec as P

HIGH = lax.Precision.HIGHEST
CORES = 2
ZLEN = 12
SUB = ("y", "z", "core")


def passed_along(block, distance, subs):
    route = [(i - distance, i) for i in range(subs) if 0 <= i - distance < subs]
    return lax.ppermute(block, SUB, route)


def body(
    right_sides, operator, local_inverse, coarse_basis, coarse_inverse, send_index, halo_count
):
    own_width = right_sides.shape[1]
    rhs_width = right_sides.shape[0]
    halo_slots = send_index.shape[3]
    n_nb = send_index.shape[2]
    n_col = lax.axis_size("col")
    ylen = lax.axis_size("y")
    subs = ylen * ZLEN * CORES
    stride = subs // 4
    offsets = (1, -1, stride, -stride)
    send_rows = send_index[0, 0]
    counts = halo_count[0, 0]
    slots = jnp.arange(halo_slots, dtype=jnp.int32)
    live_slots = (slots[None, :] < counts[:, None]).astype(jnp.float32)
    basis_rows = coarse_basis[0]
    mode_count = basis_rows.shape[1]
    block_len = basis_rows.shape[0] // n_col
    blocks_of = lambda m: m.reshape(n_col, block_len, m.shape[-1])
    operator_rows = blocks_of(operator[0])
    inverse_rows = blocks_of(local_inverse[0])
    basis_blocks = blocks_of(basis_rows)
    own_basis_all = basis_blocks[:, :own_width]
    column_index = lax.axis_index("col")
    quarter = mode_count // n_col
    own_basis = lax.dynamic_index_in_dim(own_basis_all, column_index, 0, keepdims=False)
    rows = jnp.arange(own_width, dtype=jnp.int32)
    select_own = (
        (rows[:, None, None] == send_rows[None]).astype(jnp.float32) * live_slots[None]
    ).reshape(own_width, n_nb * halo_slots)

    def pack_own(field):
        return jnp.dot(field, select_own, precision=HIGH)

    def halos(packs):
        got = [passed_along(packs[:, :, n], offsets[n], subs) for n in range(n_nb)]
        return got

    def ext_of(own_all, got):
        return jnp.concatenate([own_all] + got, axis=2)

    def apply(ext, blocks):
        return lax.dot_general(ext, blocks, (((0, 2), (0, 1)), ((), ())), precision=HIGH)

    def gathered_ext(field, extra=None):
        payload = jnp.concatenate([field, pack_own(field)], axis=1)
        if extra is not None:
            payload = jnp.concatenate([payload, extra], axis=0)
        g = lax.all_gather(payload[None], "col", axis=0, tiled=True)
        own_all = g[:, :rhs_width, :own_width]
        packs = g[:, :rhs_width, own_width:].reshape(n_col, rhs_width, n_nb, halo_slots)
        return ext_of(own_all, halos(packs)), g[:, rhs_width:]

    def coarse_partial(ext):
        coeff = apply(ext, basis_blocks)
        mine = lax.dynamic_slice_in_dim(coeff, column_index * quarter, quarter, 1).T
        spread = jnp.broadcast_to(mine[None], (ZLEN,) + mine.shape)
        g = lax.all_to_all(spread, "z", 0, 0, tiled=True)
        g = lax.all_gather(g[None], ("y", "core"), axis=0, tiled=True)
        g = g.reshape(ylen, CORES, ZLEN, quarter, rhs_width).transpose(0, 2, 1, 3, 4)
        kept_rows = g.reshape(subs * quarter, rhs_width)
        return jnp.dot(coarse_inverse, kept_rows, precision=HIGH)

    index_row = jnp.concatenate(
        [
            send_rows.reshape(-1).astype(jnp.float32),
            counts.astype(jnp.float32),
            jnp.zeros((own_width + n_nb * halo_slots - n_nb * halo_slots - n_nb,), jnp.float32),
        ]
    )[None]
    ext_b, idx = gathered_ext(right_sides, index_row)
    send_all = idx[:, 0, : n_nb * halo_slots].astype(jnp.int32).reshape(n_col, n_nb, halo_slots)
    counts_all = idx[:, 0, n_nb * halo_slots : n_nb * halo_slots + n_nb].astype(jnp.int32)
    live_all = (slots[None, None, :] < counts_all[:, :, None]).astype(jnp.float32)

    local_1 = apply(ext_b, inverse_rows)
    partial_1 = coarse_partial(ext_b)
    g = lax.all_gather(
        jnp.concatenate([local_1, partial_1.T], axis=1)[None], "col", axis=0, tiled=True
    )
    local_all = g[:, :, :own_width]
    coarse_1 = jnp.sum(g[:, :, own_width:], axis=0)
    coarse_part_all = jnp.einsum("rm,com->cro", coarse_1, own_basis_all, precision=HIGH)
    first_all = local_all + coarse_part_all
    select_all = (rows[None, :, None, None] == send_all[:, None]).astype(jnp.float32) * live_all[
        :, None
    ]
    got_first = [
        passed_along(
            lax.dot_general(
                first_all, select_all[:, :, n], (((2,), (1,)), ((0,), (0,))), precision=HIGH
            ),
            offsets[n],
            subs,
        )
        for n in range(n_nb)
    ]
    ext_f = ext_of(first_all, got_first)
    applied = apply(ext_f, operator_rows)
    residual = right_sides - applied
    first_pass = lax.dynamic_index_in_dim(first_all, column_index, 0, keepdims=False)

    ext_r, _ = gathered_ext(residual)
    local_2 = apply(ext_r, inverse_rows)
    partial_2 = coarse_partial(ext_r)
    g2 = lax.all_gather(partial_2.T[None], "col", axis=0, tiled=True)
    coarse_2 = jnp.sum(g2, axis=0)
    coarse_part_2 = lax.dot_general(
        coarse_2, own_basis, (((1,), (1,)), ((), ())), precision=HIGH
    )
    solution = first_pass + (local_2 + coarse_part_2)
    return (solution, residual)


def solution(mesh):
    subs, n_col = mesh.devices.shape
    fine = Mesh(
        mesh.devices.reshape(subs // (ZLEN * CORES), ZLEN, CORES, n_col), SUB + ("col",)
    )
    placed = (
        P(None, SUB + ("col",)),
        P(SUB, None, "col"),
        P(SUB, None, "col"),
        P(SUB, None, None),
        P(SUB, "col"),
        P(SUB, "col", None, None),
        P(SUB, "col", None),
    )
    return jax.shard_map(
        body,
        mesh=fine,
        in_specs=placed,
        out_specs=(P(None, SUB + ("col",)), P(None, SUB + ("col",))),
        check_vma=False,
    )
```

```python
import jax
import jax.numpy as jnp
from jax import lax
from jax.sharding import Mesh, PartitionSpec as P

HIGH = lax.Precision.HIGHEST
CORES = 2
ZLEN = 12
SUB = ("y", "z", "core")


def passed_along(block, distance, subs):
    route = [(i - distance, i) for i in range(subs) if 0 <= i - distance < subs]
    return lax.ppermute(block, SUB, route)


def body(
    right_sides, operator, local_inverse, coarse_basis, coarse_inverse, send_index, halo_count
):
    own_width = right_sides.shape[1]
    rhs_width = right_sides.shape[0]
    halo_slots = send_index.shape[3]
    n_nb = send_index.shape[2]
    n_col = lax.axis_size("col")
    ylen = lax.axis_size("y")
    subs = ylen * ZLEN * CORES
    stride = subs // 4
    offsets = (1, -1, stride, -stride)
    send_rows = send_index[0, 0]
    counts = halo_count[0, 0]
    slots = jnp.arange(halo_slots, dtype=jnp.int32)
    live_slots = (slots[None, :] < counts[:, None]).astype(jnp.float32)
    basis_rows = coarse_basis[0]
    mode_count = basis_rows.shape[1]
    block_len = basis_rows.shape[0] // n_col
    blocks_of = lambda m: m.reshape(n_col, block_len, m.shape[-1])
    inverse_rows = blocks_of(local_inverse[0])
    basis_blocks = blocks_of(basis_rows)
    own_basis_all = basis_blocks[:, :own_width]
    column_index = lax.axis_index("col")
    quarter = mode_count // n_col
    own_basis = lax.dynamic_index_in_dim(own_basis_all, column_index, 0, keepdims=False)
    rows = jnp.arange(own_width, dtype=jnp.int32)
    select_own = (
        (rows[:, None, None] == send_rows[None]).astype(jnp.float32) * live_slots[None]
    ).reshape(own_width, n_nb * halo_slots)

    def pack_own(field):
        return jnp.dot(field, select_own, precision=HIGH)

    def halos(packs):
        got = [passed_along(packs[:, :, n], offsets[n], subs) for n in range(n_nb)]
        return got

    def ext_of(own_all, got):
        return jnp.concatenate([own_all] + got, axis=2)

    def apply(ext, blocks):
        return lax.dot_general(ext, blocks, (((0, 2), (0, 1)), ((), ())), precision=HIGH)

    def gathered_ext(field, extra=None):
        payload = jnp.concatenate([field, pack_own(field)], axis=1)
        if extra is not None:
            payload = jnp.concatenate([payload, extra], axis=0)
        g = lax.all_gather(payload[None], "col", axis=0, tiled=True)
        own_all = g[:, :rhs_width, :own_width]
        packs = g[:, :rhs_width, own_width:].reshape(n_col, rhs_width, n_nb, halo_slots)
        return ext_of(own_all, halos(packs)), g[:, rhs_width:], own_all

    def coarse_partial(ext):
        coeff = apply(ext, basis_blocks)
        mine = lax.dynamic_slice_in_dim(coeff, column_index * quarter, quarter, 1).T
        spread = jnp.broadcast_to(mine[None], (ZLEN,) + mine.shape)
        g = lax.all_to_all(spread, "z", 0, 0, tiled=True)
        g = lax.all_gather(g[None], ("y", "core"), axis=0, tiled=True)
        g = g.reshape(ylen, CORES, ZLEN, quarter, rhs_width).transpose(0, 2, 1, 3, 4)
        kept_rows = g.reshape(subs * quarter, rhs_width)
        return jnp.dot(coarse_inverse, kept_rows, precision=HIGH)

    index_row = jnp.concatenate(
        [
            send_rows.reshape(-1).astype(jnp.float32),
            counts.astype(jnp.float32),
            jnp.zeros((own_width + n_nb * halo_slots - n_nb * halo_slots - n_nb,), jnp.float32),
        ]
    )[None]
    operator_rel = [operator[0]] + [
        lax.ppermute(operator[0], "col", [(i, (i + k) % n_col) for i in range(n_col)])
        for k in range(1, n_col)
    ]
    ext_b, idx, own_b_all = gathered_ext(right_sides, index_row)
    send_all = idx[:, 0, : n_nb * halo_slots].astype(jnp.int32).reshape(n_col, n_nb, halo_slots)
    counts_all = idx[:, 0, n_nb * halo_slots : n_nb * halo_slots + n_nb].astype(jnp.int32)
    live_all = (slots[None, None, :] < counts_all[:, :, None]).astype(jnp.float32)

    local_1 = apply(ext_b, inverse_rows)
    partial_1 = coarse_partial(ext_b)
    g = lax.all_gather(
        jnp.concatenate([local_1, partial_1.T], axis=1)[None], "col", axis=0, tiled=True
    )
    local_all = g[:, :, :own_width]
    coarse_1 = jnp.sum(g[:, :, own_width:], axis=0)
    coarse_part_all = jnp.einsum("rm,com->cro", coarse_1, own_basis_all, precision=HIGH)
    first_all = local_all + coarse_part_all
    select_all = (rows[None, :, None, None] == send_all[:, None]).astype(jnp.float32) * live_all[
        :, None
    ]
    got_first = [
        passed_along(
            lax.dot_general(
                first_all, select_all[:, :, n], (((2,), (1,)), ((0,), (0,))), precision=HIGH
            ),
            offsets[n],
            subs,
        )
        for n in range(n_nb)
    ]
    ext_f = ext_of(first_all, got_first)
    applied_rel = jnp.stack([apply(ext_f, blocks_of(m)) for m in operator_rel])
    residual = right_sides - applied_rel[0]
    back = (column_index - jnp.arange(n_col, dtype=jnp.int32)) % n_col
    residual_all = own_b_all - jnp.take(applied_rel, back, axis=0)
    first_pass = lax.dynamic_index_in_dim(first_all, column_index, 0, keepdims=False)

    got_res = [
        passed_along(
            lax.dot_general(
                residual_all, select_all[:, :, n], (((2,), (1,)), ((0,), (0,))), precision=HIGH
            ),
            offsets[n],
            subs,
        )
        for n in range(n_nb)
    ]
    ext_r = ext_of(residual_all, got_res)
    local_2 = apply(ext_r, inverse_rows)
    partial_2 = coarse_partial(ext_r)
    g2 = lax.all_gather(partial_2.T[None], "col", axis=0, tiled=True)
    coarse_2 = jnp.sum(g2, axis=0)
    coarse_part_2 = lax.dot_general(
        coarse_2, own_basis, (((1,), (1,)), ((), ())), precision=HIGH
    )
    solution = first_pass + (local_2 + coarse_part_2)
    return (solution, residual)


def solution(mesh):
    subs, n_col = mesh.devices.shape
    fine = Mesh(
        mesh.devices.reshape(subs // (ZLEN * CORES), ZLEN, CORES, n_col), SUB + ("col",)
    )
    placed = (
        P(None, SUB + ("col",)),
        P(SUB, None, "col"),
        P(SUB, None, "col"),
        P(SUB, None, None),
        P(SUB, "col"),
        P(SUB, "col", None, None),
        P(SUB, "col", None),
    )
    return jax.shard_map(
        body,
        mesh=fine,
        in_specs=placed,
        out_specs=(P(None, SUB + ("col",)), P(None, SUB + ("col",))),
        check_vma=False,
    )
```

```python
import jax
import jax.numpy as jnp
from jax import lax
from jax.sharding import Mesh, PartitionSpec as P

HIGH = lax.Precision.HIGHEST
CORES = 2
ZLEN = 12
SUB = ("y", "z", "core")


def passed_along(block, distance, subs):
    route = [(i - distance, i) for i in range(subs) if 0 <= i - distance < subs]
    return lax.ppermute(block, SUB, route)


def body(
    right_sides, operator, local_inverse, coarse_basis, coarse_inverse, send_index, halo_count
):
    own_width = right_sides.shape[1]
    rhs_width = right_sides.shape[0]
    halo_slots = send_index.shape[3]
    n_nb = send_index.shape[2]
    n_col = lax.axis_size("col")
    ylen = lax.axis_size("y")
    subs = ylen * ZLEN * CORES
    stride = subs // 4
    offsets = (1, -1, stride, -stride)
    send_rows = send_index[0, 0]
    counts = halo_count[0, 0]
    slots = jnp.arange(halo_slots, dtype=jnp.int32)
    basis_rows = coarse_basis[0]
    mode_count = basis_rows.shape[1]
    block_len = basis_rows.shape[0] // n_col
    blocks_of = lambda m: m.reshape(n_col, block_len, m.shape[-1])
    operator_rows = blocks_of(operator[0])
    inverse_rows = blocks_of(local_inverse[0])
    basis_blocks = blocks_of(basis_rows)
    own_basis_all = basis_blocks[:, :own_width]
    column_index = lax.axis_index("col")
    quarter = mode_count // n_col
    own_basis = lax.dynamic_index_in_dim(own_basis_all, column_index, 0, keepdims=False)
    rows = jnp.arange(own_width, dtype=jnp.int32)

    def ext_of(own_all, got):
        return jnp.concatenate([own_all] + got, axis=2)

    def apply(ext, blocks):
        return lax.dot_general(ext, blocks, (((0, 2), (0, 1)), ((), ())), precision=HIGH)

    def coarse_partial(ext):
        coeff = apply(ext, basis_blocks)
        mine = lax.dynamic_slice_in_dim(coeff, column_index * quarter, quarter, 1).T
        spread = jnp.broadcast_to(mine[None], (ZLEN,) + mine.shape)
        g = lax.all_to_all(spread, "z", 0, 0, tiled=True)
        g = lax.all_gather(g[None], ("y", "core"), axis=0, tiled=True)
        g = g.reshape(ylen, CORES, ZLEN, quarter, rhs_width).transpose(0, 2, 1, 3, 4)
        kept_rows = g.reshape(subs * quarter, rhs_width)
        return jnp.dot(coarse_inverse, kept_rows, precision=HIGH)

    index_row = jnp.concatenate(
        [
            send_rows.reshape(-1).astype(jnp.float32),
            counts.astype(jnp.float32),
            jnp.zeros((own_width - n_nb * halo_slots - n_nb,), jnp.float32),
        ]
    )[None]
    g0 = lax.all_gather(
        jnp.concatenate([right_sides, index_row], axis=0)[None], "col", axis=0, tiled=True
    )
    own_b_all = g0[:, :rhs_width]
    idx = g0[:, rhs_width]
    send_all = idx[:, : n_nb * halo_slots].astype(jnp.int32).reshape(n_col, n_nb, halo_slots)
    counts_all = idx[:, n_nb * halo_slots : n_nb * halo_slots + n_nb].astype(jnp.int32)
    live_all = (slots[None, None, :] < counts_all[:, :, None]).astype(jnp.float32)
    select_all = (rows[None, :, None, None] == send_all[:, None]).astype(jnp.float32) * live_all[
        :, None
    ]

    def margins_sent(field_all):
        return [
            passed_along(
                lax.dot_general(
                    field_all, select_all[:, :, n], (((2,), (1,)), ((0,), (0,))), precision=HIGH
                ),
                offsets[n],
                subs,
            )
            for n in range(n_nb)
        ]

    ext_b = ext_of(own_b_all, margins_sent(own_b_all))

    local_1 = apply(ext_b, inverse_rows)
    partial_1 = coarse_partial(ext_b)
    g = lax.all_gather(
        jnp.concatenate([local_1, partial_1.T], axis=1)[None], "col", axis=0, tiled=True
    )
    local_all = g[:, :, :own_width]
    coarse_1 = jnp.sum(g[:, :, own_width:], axis=0)
    coarse_part_all = jnp.einsum("rm,com->cro", coarse_1, own_basis_all, precision=HIGH)
    first_all = local_all + coarse_part_all
    got_first = margins_sent(first_all)
    ext_f = ext_of(first_all, got_first)
    applied = apply(ext_f, operator_rows)
    residual = right_sides - applied
    first_pass = lax.dynamic_index_in_dim(first_all, column_index, 0, keepdims=False)

    res_all = lax.all_gather(residual[None], "col", axis=0, tiled=True)
    got_res = margins_sent(res_all)
    ext_r = ext_of(res_all, got_res)
    local_2 = apply(ext_r, inverse_rows)
    partial_2 = coarse_partial(ext_r)
    g2 = lax.all_gather(partial_2.T[None], "col", axis=0, tiled=True)
    coarse_2 = jnp.sum(g2, axis=0)
    coarse_part_2 = lax.dot_general(
        coarse_2, own_basis, (((1,), (1,)), ((), ())), precision=HIGH
    )
    solution = first_pass + (local_2 + coarse_part_2)
    return (solution, residual)


def solution(mesh):
    subs, n_col = mesh.devices.shape
    fine = Mesh(
        mesh.devices.reshape(subs // (ZLEN * CORES), ZLEN, CORES, n_col), SUB + ("col",)
    )
    placed = (
        P(None, SUB + ("col",)),
        P(SUB, None, "col"),
        P(SUB, None, "col"),
        P(SUB, None, None),
        P(SUB, "col"),
        P(SUB, "col", None, None),
        P(SUB, "col", None),
    )
    return jax.shard_map(
        body,
        mesh=fine,
        in_specs=placed,
        out_specs=(P(None, SUB + ("col",)), P(None, SUB + ("col",))),
        check_vma=False,
    )
```

```python
import jax
import jax.numpy as jnp
from jax import lax
from jax.sharding import Mesh, PartitionSpec as P

HIGH = lax.Precision.HIGHEST
CORES = 2
ZLEN = 12
SUB = ("y", "z", "core")


def passed_along(block, distance, subs):
    route = [(i - distance, i) for i in range(subs) if 0 <= i - distance < subs]
    return lax.ppermute(block, SUB, route)


def body(
    right_sides, operator, local_inverse, coarse_basis, coarse_inverse, send_index, halo_count
):
    own_width = right_sides.shape[1]
    rhs_width = right_sides.shape[0]
    halo_slots = send_index.shape[3]
    n_nb = send_index.shape[2]
    n_col = lax.axis_size("col")
    ylen = lax.axis_size("y")
    subs = ylen * ZLEN * CORES
    stride = subs // 4
    offsets = (1, -1, stride, -stride)
    send_rows = send_index[0, 0]
    counts = halo_count[0, 0]
    slots = jnp.arange(halo_slots, dtype=jnp.int32)
    basis_rows = coarse_basis[0]
    mode_count = basis_rows.shape[1]
    block_len = basis_rows.shape[0] // n_col
    blocks_of = lambda m: m.reshape(n_col, block_len, m.shape[-1])
    operator_rows = blocks_of(operator[0])
    inverse_rows = blocks_of(local_inverse[0])
    basis_blocks = blocks_of(basis_rows)
    own_basis_all = basis_blocks[:, :own_width]
    column_index = lax.axis_index("col")
    quarter = mode_count // n_col
    own_basis = lax.dynamic_index_in_dim(own_basis_all, column_index, 0, keepdims=False)
    rows = jnp.arange(own_width, dtype=jnp.int32)

    def ext_of(own_all, got):
        return (own_all, got)

    def contract(part, rows_of):
        return lax.dot_general(part, rows_of, (((0, 2), (0, 1)), ((), ())), precision=HIGH)

    def apply(ext, blocks):
        own_all, got = ext
        total = contract(own_all, blocks[:, :own_width])
        for n in range(n_nb):
            low = own_width + n * halo_slots
            total = total + contract(got[n], blocks[:, low : low + halo_slots])
        return total

    def coarse_partial(ext):
        coeff = apply(ext, basis_blocks)
        mine = lax.dynamic_slice_in_dim(coeff, column_index * quarter, quarter, 1).T
        spread = jnp.broadcast_to(mine[None], (ZLEN,) + mine.shape)
        g = lax.all_to_all(spread, "z", 0, 0, tiled=True)
        g = lax.all_gather(g[None], ("y", "core"), axis=0, tiled=True)
        g = g.reshape(ylen, CORES, ZLEN, quarter, rhs_width).transpose(0, 2, 1, 3, 4)
        kept_rows = g.reshape(subs * quarter, rhs_width)
        return jnp.dot(coarse_inverse, kept_rows, precision=HIGH)

    index_row = jnp.concatenate(
        [
            send_rows.reshape(-1).astype(jnp.float32),
            counts.astype(jnp.float32),
            jnp.zeros((own_width - n_nb * halo_slots - n_nb,), jnp.float32),
        ]
    )[None]
    g0 = lax.all_gather(
        jnp.concatenate([right_sides, index_row], axis=0)[None], "col", axis=0, tiled=True
    )
    own_b_all = g0[:, :rhs_width]
    idx = g0[:, rhs_width]
    send_all = idx[:, : n_nb * halo_slots].astype(jnp.int32).reshape(n_col, n_nb, halo_slots)
    counts_all = idx[:, n_nb * halo_slots : n_nb * halo_slots + n_nb].astype(jnp.int32)
    live_all = (slots[None, None, :] < counts_all[:, :, None]).astype(jnp.float32)
    select_all = (rows[None, :, None, None] == send_all[:, None]).astype(jnp.float32) * live_all[
        :, None
    ]

    def margins_sent(field_all):
        return [
            passed_along(
                lax.dot_general(
                    field_all, select_all[:, :, n], (((2,), (1,)), ((0,), (0,))), precision=HIGH
                ),
                offsets[n],
                subs,
            )
            for n in range(n_nb)
        ]

    ext_b = ext_of(own_b_all, margins_sent(own_b_all))

    local_1 = apply(ext_b, inverse_rows)
    partial_1 = coarse_partial(ext_b)
    g = lax.all_gather(
        jnp.concatenate([local_1, partial_1.T], axis=1)[None], "col", axis=0, tiled=True
    )
    local_all = g[:, :, :own_width]
    coarse_1 = jnp.sum(g[:, :, own_width:], axis=0)
    coarse_part_all = jnp.einsum("rm,com->cro", coarse_1, own_basis_all, precision=HIGH)
    first_all = local_all + coarse_part_all
    got_first = margins_sent(first_all)
    ext_f = ext_of(first_all, got_first)
    applied = apply(ext_f, operator_rows)
    residual = right_sides - applied
    first_pass = lax.dynamic_index_in_dim(first_all, column_index, 0, keepdims=False)

    res_all = lax.all_gather(residual[None], "col", axis=0, tiled=True)
    got_res = margins_sent(res_all)
    ext_r = ext_of(res_all, got_res)
    local_2 = apply(ext_r, inverse_rows)
    partial_2 = coarse_partial(ext_r)
    g2 = lax.all_gather(partial_2.T[None], "col", axis=0, tiled=True)
    coarse_2 = jnp.sum(g2, axis=0)
    coarse_part_2 = lax.dot_general(
        coarse_2, own_basis, (((1,), (1,)), ((), ())), precision=HIGH
    )
    solution = first_pass + (local_2 + coarse_part_2)
    return (solution, residual)


def solution(mesh):
    subs, n_col = mesh.devices.shape
    fine = Mesh(
        mesh.devices.reshape(subs // (ZLEN * CORES), ZLEN, CORES, n_col), SUB + ("col",)
    )
    placed = (
        P(None, SUB + ("col",)),
        P(SUB, None, "col"),
        P(SUB, None, "col"),
        P(SUB, None, None),
        P(SUB, "col"),
        P(SUB, "col", None, None),
        P(SUB, "col", None),
    )
    return jax.shard_map(
        body,
        mesh=fine,
        in_specs=placed,
        out_specs=(P(None, SUB + ("col",)), P(None, SUB + ("col",))),
        check_vma=False,
    )
```

```python
import jax
import jax.numpy as jnp
from jax import lax
from jax.sharding import Mesh, PartitionSpec as P

HIGH = lax.Precision.HIGHEST
CORES = 2
ZLEN = 12
SUB = ("y", "z", "core")


def passed_along(block, distance, subs):
    route = [(i - distance, i) for i in range(subs) if 0 <= i - distance < subs]
    return lax.ppermute(block, SUB, route)


def body(
    right_sides, operator, local_inverse, coarse_basis, coarse_inverse, send_index, halo_count
):
    own_width = right_sides.shape[1]
    rhs_width = right_sides.shape[0]
    halo_slots = send_index.shape[3]
    n_nb = send_index.shape[2]
    n_col = lax.axis_size("col")
    ylen = lax.axis_size("y")
    subs = ylen * ZLEN * CORES
    stride = subs // 4
    offsets = (1, -1, stride, -stride)
    send_rows = send_index[0, 0]
    counts = halo_count[0, 0]
    slots = jnp.arange(halo_slots, dtype=jnp.int32)
    basis_rows = coarse_basis[0]
    mode_count = basis_rows.shape[1]
    block_len = basis_rows.shape[0] // n_col
    blocks_of = lambda m: m.reshape(n_col, block_len, m.shape[-1])
    operator_rows = blocks_of(operator[0])
    inverse_rows = blocks_of(local_inverse[0])
    basis_blocks = blocks_of(basis_rows)
    own_basis_all = basis_blocks[:, :own_width]
    column_index = lax.axis_index("col")
    quarter = mode_count // n_col
    own_basis = lax.dynamic_index_in_dim(own_basis_all, column_index, 0, keepdims=False)
    rows = jnp.arange(own_width, dtype=jnp.int32)

    def col_gather(part):
        spread = jnp.broadcast_to(part, (n_col,) + part.shape[1:])
        return lax.all_to_all(spread, "col", 0, 0, tiled=True)

    def ext_of(own_all, got):
        return jnp.concatenate([own_all] + got, axis=2)

    def apply(ext, blocks):
        return lax.dot_general(ext, blocks, (((0, 2), (0, 1)), ((), ())), precision=HIGH)

    def coarse_partial(ext):
        coeff = apply(ext, basis_blocks)
        mine = lax.dynamic_slice_in_dim(coeff, column_index * quarter, quarter, 1).T
        spread = jnp.broadcast_to(mine[None], (ZLEN,) + mine.shape)
        g = lax.all_to_all(spread, "z", 0, 0, tiled=True)
        g = lax.all_gather(g[None], ("y", "core"), axis=0, tiled=True)
        g = g.reshape(ylen, CORES, ZLEN, quarter, rhs_width).transpose(0, 2, 1, 3, 4)
        kept_rows = g.reshape(subs * quarter, rhs_width)
        return jnp.dot(coarse_inverse, kept_rows, precision=HIGH)

    index_row = jnp.concatenate(
        [
            send_rows.reshape(-1).astype(jnp.float32),
            counts.astype(jnp.float32),
            jnp.zeros((own_width - n_nb * halo_slots - n_nb,), jnp.float32),
        ]
    )[None]
    g0 = col_gather(jnp.concatenate([right_sides, index_row], axis=0)[None])
    own_b_all = g0[:, :rhs_width]
    idx = g0[:, rhs_width]
    send_all = idx[:, : n_nb * halo_slots].astype(jnp.int32).reshape(n_col, n_nb, halo_slots)
    counts_all = idx[:, n_nb * halo_slots : n_nb * halo_slots + n_nb].astype(jnp.int32)
    live_all = (slots[None, None, :] < counts_all[:, :, None]).astype(jnp.float32)
    select_all = (rows[None, :, None, None] == send_all[:, None]).astype(jnp.float32) * live_all[
        :, None
    ]

    def margins_sent(field_all):
        return [
            passed_along(
                lax.dot_general(
                    field_all, select_all[:, :, n], (((2,), (1,)), ((0,), (0,))), precision=HIGH
                ),
                offsets[n],
                subs,
            )
            for n in range(n_nb)
        ]

    ext_b = ext_of(own_b_all, margins_sent(own_b_all))

    local_1 = apply(ext_b, inverse_rows)
    partial_1 = coarse_partial(ext_b)
    g = col_gather(jnp.concatenate([local_1, partial_1.T], axis=1)[None])
    local_all = g[:, :, :own_width]
    coarse_1 = jnp.sum(g[:, :, own_width:], axis=0)
    coarse_part_all = jnp.einsum("rm,com->cro", coarse_1, own_basis_all, precision=HIGH)
    first_all = local_all + coarse_part_all
    got_first = margins_sent(first_all)
    ext_f = ext_of(first_all, got_first)
    applied = apply(ext_f, operator_rows)
    residual = right_sides - applied
    first_pass = lax.dynamic_index_in_dim(first_all, column_index, 0, keepdims=False)

    res_all = col_gather(residual[None])
    got_res = margins_sent(res_all)
    ext_r = ext_of(res_all, got_res)
    local_2 = apply(ext_r, inverse_rows)
    partial_2 = coarse_partial(ext_r)
    g2 = col_gather(partial_2.T[None])
    coarse_2 = jnp.sum(g2, axis=0)
    coarse_part_2 = lax.dot_general(
        coarse_2, own_basis, (((1,), (1,)), ((), ())), precision=HIGH
    )
    solution = first_pass + (local_2 + coarse_part_2)
    return (solution, residual)


def solution(mesh):
    subs, n_col = mesh.devices.shape
    fine = Mesh(
        mesh.devices.reshape(subs // (ZLEN * CORES), ZLEN, CORES, n_col), SUB + ("col",)
    )
    placed = (
        P(None, SUB + ("col",)),
        P(SUB, None, "col"),
        P(SUB, None, "col"),
        P(SUB, None, None),
        P(SUB, "col"),
        P(SUB, "col", None, None),
        P(SUB, "col", None),
    )
    return jax.shard_map(
        body,
        mesh=fine,
        in_specs=placed,
        out_specs=(P(None, SUB + ("col",)), P(None, SUB + ("col",))),
        check_vma=False,
    )
```

```python
import jax
import jax.numpy as jnp
from jax import lax
from jax.sharding import Mesh, PartitionSpec as P

HIGH = lax.Precision.HIGHEST
CORES = 2
ZLEN = 12
SUB = ("y", "z", "core")


def passed_along(block, distance, subs):
    route = [(i - distance, i) for i in range(subs) if 0 <= i - distance < subs]
    return lax.ppermute(block, SUB, route)


def body(
    right_sides, operator, local_inverse, coarse_basis, coarse_inverse, send_index, halo_count
):
    own_width = right_sides.shape[1]
    rhs_width = right_sides.shape[0]
    halo_slots = send_index.shape[3]
    n_nb = send_index.shape[2]
    n_col = lax.axis_size("col")
    ylen = lax.axis_size("y")
    subs = ylen * ZLEN * CORES
    stride = subs // 4
    offsets = (1, -1, stride, -stride)
    send_rows = send_index[0, 0]
    counts = halo_count[0, 0]
    slots = jnp.arange(halo_slots, dtype=jnp.int32)
    basis_rows = coarse_basis[0]
    mode_count = basis_rows.shape[1]
    block_len = basis_rows.shape[0] // n_col
    blocks_of = lambda m: m.reshape(n_col, block_len, m.shape[-1])
    operator_rows = blocks_of(operator[0])
    inverse_rows = blocks_of(local_inverse[0])
    basis_blocks = blocks_of(basis_rows)
    own_basis_all = basis_blocks[:, :own_width]
    column_index = lax.axis_index("col")
    quarter = mode_count // n_col
    own_basis = lax.dynamic_index_in_dim(own_basis_all, column_index, 0, keepdims=False)
    rows = jnp.arange(own_width, dtype=jnp.int32)

    def col_gather(part):
        spread = jnp.broadcast_to(part, (n_col,) + part.shape[1:])
        return lax.all_to_all(spread, "col", 0, 0, tiled=True)

    def ext_of(own_all, got):
        return jnp.concatenate([own_all] + got, axis=2)

    def apply(ext, blocks):
        return lax.dot_general(ext, blocks, (((0, 2), (0, 1)), ((), ())), precision=HIGH)

    def coarse_partial(ext):
        coeff = apply(ext, basis_blocks)
        mine = lax.dynamic_slice_in_dim(coeff, column_index * quarter, quarter, 1).T
        spread = jnp.broadcast_to(mine[None], (ZLEN,) + mine.shape)
        g = lax.all_to_all(spread, "z", 0, 0, tiled=True)
        g = lax.all_gather(g[None], ("y", "core"), axis=0, tiled=True)
        g = g.reshape(ylen, CORES, ZLEN, quarter, rhs_width).transpose(0, 2, 1, 3, 4)
        kept_rows = g.reshape(subs * quarter, rhs_width)
        return jnp.dot(coarse_inverse, kept_rows, precision=HIGH)

    index_all = lax.all_gather(
        jnp.concatenate([send_rows.reshape(-1), counts])[None], "col", axis=0, tiled=True
    )
    own_b_all = col_gather(right_sides[None])
    send_all = index_all[:, : n_nb * halo_slots].reshape(n_col, n_nb, halo_slots)
    counts_all = index_all[:, n_nb * halo_slots : n_nb * halo_slots + n_nb]
    live_all = (slots[None, None, :] < counts_all[:, :, None]).astype(jnp.float32)
    select_all = (rows[None, :, None, None] == send_all[:, None]).astype(jnp.float32) * live_all[
        :, None
    ]

    def margins_sent(field_all):
        return [
            passed_along(
                lax.dot_general(
                    field_all, select_all[:, :, n], (((2,), (1,)), ((0,), (0,))), precision=HIGH
                ),
                offsets[n],
                subs,
            )
            for n in range(n_nb)
        ]

    ext_b = ext_of(own_b_all, margins_sent(own_b_all))

    local_1 = apply(ext_b, inverse_rows)
    partial_1 = coarse_partial(ext_b)
    g = col_gather(jnp.concatenate([local_1, partial_1.T], axis=1)[None])
    local_all = g[:, :, :own_width]
    coarse_1 = jnp.sum(g[:, :, own_width:], axis=0)
    coarse_part_all = jnp.einsum("rm,com->cro", coarse_1, own_basis_all, precision=HIGH)
    first_all = local_all + coarse_part_all
    got_first = margins_sent(first_all)
    ext_f = ext_of(first_all, got_first)
    applied = apply(ext_f, operator_rows)
    residual = right_sides - applied
    first_pass = lax.dynamic_index_in_dim(first_all, column_index, 0, keepdims=False)

    res_all = col_gather(residual[None])
    got_res = margins_sent(res_all)
    ext_r = ext_of(res_all, got_res)
    local_2 = apply(ext_r, inverse_rows)
    partial_2 = coarse_partial(ext_r)
    g2 = col_gather(partial_2.T[None])
    coarse_2 = jnp.sum(g2, axis=0)
    coarse_part_2 = lax.dot_general(
        coarse_2, own_basis, (((1,), (1,)), ((), ())), precision=HIGH
    )
    solution = first_pass + (local_2 + coarse_part_2)
    return (solution, residual)


def solution(mesh):
    subs, n_col = mesh.devices.shape
    fine = Mesh(
        mesh.devices.reshape(subs // (ZLEN * CORES), ZLEN, CORES, n_col), SUB + ("col",)
    )
    placed = (
        P(None, SUB + ("col",)),
        P(SUB, None, "col"),
        P(SUB, None, "col"),
        P(SUB, None, None),
        P(SUB, "col"),
        P(SUB, "col", None, None),
        P(SUB, "col", None),
    )
    return jax.shard_map(
        body,
        mesh=fine,
        in_specs=placed,
        out_specs=(P(None, SUB + ("col",)), P(None, SUB + ("col",))),
        check_vma=False,
    )
```
